128 devices in a mesh: tm: 8 (over x, core), pts: 16 (over z, y).
Axes of the slice: x: 4, y: 4, z: 4, core: 2. Of those that a mesh axis runs over, the one named last changes fastest.
Arguments:
- base_grid: float32 [12, 256, 16384], P(None, 'tm', 'pts'), may hold values from -5 to 5
- sample_index: int32 [8192], P('pts'), may hold values from 0 to 1023, as said below
- exponents: int32 [512, 12], replicated, may hold values from 0 to 3, as said below
Outputs:
- gram: float32 [512, 512], P('pts', 'tm')
- cross: float32 [3, 512], P(None, 'pts')
The draws below stay inside these ranges and needn't reach their ends.
Inputs may be any that keep to these rules, and one draw needn't show every extreme that they name: `sample_index`: within one index of pts the sampled cells are distinct, and each is below 1024. `exponents`: every term has total degree at most 3.
All inputs are finite; a program needn't handle non-finite values.
Results may differ from the reference program's by a relative error of at most 0.00034.
Values sent between devices are 32-bit elements; how exact they have to be, the bound alone decides.
No kernel may reach another device: no remote copies, remote signals or barrier semaphores. Data moves between devices by JAX's collectives and lax.ppermute only.
A program may use at most 192 MiB of HBM per device.

```python
import jax
import jax.numpy as jnp
from jax import lax

TERMS = 512
FIELDS = 12
TARGETS = 3
PTS_DEV = 512
GRID_DEV = 1024
TIMES = 256
SAMPLES = 8192
CELLS = 16384
N_PTS = 16


def draw_sample_index(key, part):
    keys = jax.random.split(jax.random.fold_in(key, 11), N_PTS)

    def one_block(block_key):
        picked = jax.random.permutation(block_key, GRID_DEV - 1)[:PTS_DEV - 1].astype(jnp.int32)
        return jnp.concatenate([picked, jnp.array([GRID_DEV - 1], jnp.int32)])
    return jax.vmap(one_block)(keys).reshape(-1).astype(jnp.int32)


def draw_exponents(key, part):
    key_slots, key_live = jax.random.split(jax.random.fold_in(key, 23))
    slots = jax.random.randint(key_slots, (TERMS, 3), 0, FIELDS).astype(jnp.int32)
    live = (jax.random.randint(key_live, (TERMS, 3), 0, 4) > 0).astype(jnp.int32)
    forced = (jnp.arange(TERMS) % 64 == 0)[:, None]
    slots = jnp.where(forced, slots[:, :1], slots)
    live = jnp.where(forced, 1, live)
    hits = (slots[:, :, None] == jnp.arange(FIELDS)[None, None, :]).astype(jnp.int32)
    return jnp.sum(hits * live[:, :, None], axis=1).astype(jnp.int32)


def level_of(own_key, extent, cuts, smallest, top_value):
    def one(position, parts):
        steps = jax.random.uniform(jax.random.fold_in(jax.random.fold_in(own_key, 6), position), (parts,), jnp.float32, smallest / len(cuts), top_value / len(cuts))
        return jnp.repeat(jnp.exp(steps), extent[position] // parts).reshape((-1,) + (1,) * (len(extent) - position - 1))

    gain = one(*cuts[0])
    for cut in cuts[1:]:
        gain = gain * one(*cut)
    return gain


def normal_values(own_key, extent, deviation, limit, shards=(), dtype=jnp.bfloat16):
    drawn = jax.random.normal(own_key, extent, jnp.float32) * deviation
    if len(shards) > 0:
        drawn = level_of(own_key, extent, shards, -0.22, 0.18) * drawn
    return jnp.clip(drawn, min=-limit, max=limit).astype(dtype)


def setup_inputs(seed: int = 0) -> dict:
    splits = jax.random.split(jax.random.key(seed), 4)
    return {
        "base_grid": normal_values(splits[0], (FIELDS, TIMES, CELLS), 0.8, 5.0, ((1, 8), (2, 16)), jnp.float32),
        "sample_index": draw_sample_index(jax.random.fold_in(splits[3], 71), 0),
        "exponents": draw_exponents(jax.random.fold_in(splits[3], 71), 0),
    }


def monomials(piece, exponents):
    theta = jnp.ones((exponents.shape[0],) + piece.shape[1:], jnp.float32)
    for field in range(piece.shape[0]):
        value = piece[field][None]
        square = value * value
        power = exponents[:, field][:, None, None]
        factor = jnp.where(power == 0, jnp.float32(1.0), jnp.where(power == 1, value, jnp.where(power == 2, square, square * value)))
        theta = theta * factor
    return theta


def reference(base_grid, sample_index, exponents):
    owner = (jnp.arange(SAMPLES) // PTS_DEV).astype(jnp.int32)
    cells = (sample_index + owner * GRID_DEV).astype(jnp.int32)
    sampled = jnp.take(base_grid, cells, axis=2)
    width = min(64, SAMPLES)
    count = SAMPLES // width
    pieces = jnp.transpose(sampled.reshape(FIELDS, TIMES, count, width), (2, 0, 1, 3))
    scale = jnp.float32(1.0 / TIMES)

    def step(carry, piece):
        gram_acc, cross_acc = carry
        theta = monomials(piece, exponents)
        running = jnp.cumsum(theta, axis=1)
        before = jnp.concatenate([jnp.zeros_like(running[:, :1]), running[:, :-1]], axis=1)
        integral = (before * scale).astype(jnp.bfloat16).reshape(TERMS, TIMES * width)
        increment = (piece[:TARGETS] - piece[:TARGETS, :1]).astype(jnp.bfloat16).reshape(TARGETS, TIMES * width)
        gram_acc = gram_acc + jnp.dot(integral, integral.T, preferred_element_type=jnp.float32)
        cross_acc = cross_acc + jnp.dot(increment, integral.T, preferred_element_type=jnp.float32)
        return (gram_acc, cross_acc), None

    start = (jnp.zeros((TERMS, TERMS), jnp.float32), jnp.zeros((TARGETS, TERMS), jnp.float32))
    (gram_acc, cross_acc), unused = lax.scan(step, start, pieces)
    norm = jnp.float32(1.0 / (TIMES * SAMPLES))
    return gram_acc * norm, cross_acc * norm
```

```python
import jax
import jax.numpy as jnp
from jax import lax
from jax.sharding import PartitionSpec as P


def factor_indices(exponents):
    running = jnp.cumsum(exponents, axis=1)
    picks = [jnp.sum((running <= j).astype(jnp.int32), axis=1) for j in range(3)]
    squared_last = (picks[1] == picks[2]) & (picks[0] != picks[1])
    return picks, squared_last


def shards(base_grid, sample_index, exponents):
    fields, snaps, unused_cells = base_grid.shape
    points = sample_index.shape[0]
    terms = exponents.shape[0]
    targets = 3
    time_devices = lax.axis_size("tm")
    point_devices = lax.axis_size("pts")
    all_snaps = snaps * time_devices
    own = points // time_devices

    sampled = jnp.take(base_grid, sample_index, axis=2)
    sampled = lax.all_to_all(sampled, "tm", 2, 1, tiled=True)
    series = jnp.transpose(sampled, (0, 2, 1))
    ones = jnp.ones((1, own, all_snaps), jnp.float32)
    table = jnp.concatenate([series, ones], axis=0)

    picks, squared_last = factor_indices(exponents)
    first, second, third = [jnp.take(table, pick, axis=0) for pick in picks]
    theta = jnp.where(
        squared_last[:, None, None], first * (second * third), (first * second) * third
    )

    before = jnp.arange(all_snaps)[:, None] < jnp.arange(all_snaps)[None, :]
    upper = jnp.where(before, 1.0 / all_snaps, 0.0).astype(jnp.bfloat16)
    high = theta.astype(jnp.bfloat16)
    rest = theta - high.astype(jnp.float32)
    middle = rest.astype(jnp.bfloat16)
    low = (rest - middle.astype(jnp.float32)).astype(jnp.bfloat16)
    contract_time = (((2,), (0,)), ((), ()))
    running = (
        lax.dot_general(high, upper, contract_time, preferred_element_type=jnp.float32)
        + lax.dot_general(middle, upper, contract_time, preferred_element_type=jnp.float32)
        + lax.dot_general(low, upper, contract_time, preferred_element_type=jnp.float32)
    )
    integral = running.astype(jnp.bfloat16)

    increment = (series[:targets] - series[:targets, :, :1]).astype(jnp.bfloat16)
    contract = (((1, 2), (1, 2)), ((), ()))
    gram_part = lax.dot_general(integral, integral, contract, preferred_element_type=jnp.float32)
    cross_part = lax.dot_general(increment, integral, contract, preferred_element_type=jnp.float32)

    row_span = terms // point_devices
    col_span = terms // time_devices
    blocks = gram_part.reshape(point_devices, row_span, time_devices, col_span)
    blocks = jnp.transpose(blocks, (0, 2, 1, 3)).reshape(point_devices, time_devices, -1)
    cross_blocks = jnp.transpose(cross_part.reshape(targets, point_devices, row_span), (1, 0, 2))
    cross_blocks = jnp.broadcast_to(
        cross_blocks.reshape(point_devices, 1, -1), (point_devices, time_devices, targets * row_span)
    )
    packed = jnp.concatenate([blocks, cross_blocks], axis=2)
    mine = lax.psum_scatter(packed, "pts", scatter_dimension=0, tiled=True)[0]
    mine = lax.psum_scatter(mine, "tm", scatter_dimension=0, tiled=True)
    norm = jnp.float32(1.0 / (all_snaps * points * point_devices))
    mine = mine[0] * norm
    gram_own = mine[: row_span * col_span].reshape(row_span, col_span)
    cross_own = mine[row_span * col_span :].reshape(targets, row_span)
    return (gram_own, cross_own)


def solution(mesh):
    return jax.shard_map(
        shards,
        mesh=mesh,
        in_specs=(P(None, "tm", "pts"), P("pts"), P()),
        out_specs=(P("pts", "tm"), P(None, "pts")),
        check_vma=False,
    )
```

```python
import jax
import jax.numpy as jnp
from jax import lax
from jax.experimental import pallas as pl
from jax.experimental.pallas import tpu as pltpu
from jax.sharding import PartitionSpec as P


def factor_indices(exponents):
    running = jnp.cumsum(exponents, axis=1)
    picks = [jnp.sum((running <= j).astype(jnp.int32), axis=1) for j in range(3)]
    squared_last = (picks[1] == picks[2]) & (picks[0] != picks[1])
    ordered = [
        jnp.where(squared_last, picks[1], picks[0]),
        jnp.where(squared_last, picks[2], picks[1]),
        jnp.where(squared_last, picks[0], picks[2]),
    ]
    return jnp.stack(ordered)


def integral_kernel(picks_ref, table_ref, upper_ref, out_ref, high_ref, middle_ref, low_ref):
    block = pl.program_id(0)
    own = table_ref.shape[1]
    count = out_ref.shape[0] // own
    for j in range(count):
        term = block * count + j
        theta = (table_ref[picks_ref[0, term]] * table_ref[picks_ref[1, term]]) * table_ref[
            picks_ref[2, term]
        ]
        high = theta.astype(jnp.bfloat16)
        rest = theta - high.astype(jnp.float32)
        middle = rest.astype(jnp.bfloat16)
        low = (rest - middle.astype(jnp.float32)).astype(jnp.bfloat16)
        rows = pl.ds(j * own, own)
        high_ref[rows, :] = high
        middle_ref[rows, :] = middle
        low_ref[rows, :] = low
    upper = upper_ref[...]
    out = jnp.dot(high_ref[...], upper, preferred_element_type=jnp.float32)
    out = out + jnp.dot(middle_ref[...], upper, preferred_element_type=jnp.float32)
    out = out + jnp.dot(low_ref[...], upper, preferred_element_type=jnp.float32)
    out_ref[...] = out.astype(jnp.bfloat16)


def integral_of(table, picks, upper, terms, per_step=16):
    width, own, snaps = table.shape
    rows = per_step * own
    return pl.pallas_call(
        integral_kernel,
        out_shape=jax.ShapeDtypeStruct((terms * own, snaps), jnp.bfloat16),
        grid_spec=pltpu.PrefetchScalarGridSpec(
            num_scalar_prefetch=1,
            grid=(terms // per_step,),
            in_specs=[
                pl.BlockSpec((width, own, snaps), lambda i, picks: (0, 0, 0)),
                pl.BlockSpec((snaps, snaps), lambda i, picks: (0, 0)),
            ],
            out_specs=pl.BlockSpec((rows, snaps), lambda i, picks: (i, 0)),
            scratch_shapes=[pltpu.VMEM((rows, snaps), jnp.bfloat16) for _ in range(3)],
        ),
        compiler_params=pltpu.CompilerParams(dimension_semantics=("arbitrary",)),
    )(picks, table, upper).reshape(terms, own, snaps)


def shards(base_grid, sample_index, exponents):
    fields, snaps, unused_cells = base_grid.shape
    points = sample_index.shape[0]
    terms = exponents.shape[0]
    targets = 3
    time_devices = lax.axis_size("tm")
    point_devices = lax.axis_size("pts")
    all_snaps = snaps * time_devices
    own = points // time_devices

    sampled = jnp.take(base_grid, sample_index, axis=2)
    sampled = lax.all_to_all(sampled, "tm", 2, 1, tiled=True)
    series = jnp.transpose(sampled, (0, 2, 1))
    ones = jnp.ones((1, own, all_snaps), jnp.float32)
    table = jnp.concatenate([series, ones], axis=0)

    picks = factor_indices(exponents)
    before = jnp.arange(all_snaps)[:, None] < jnp.arange(all_snaps)[None, :]
    upper = jnp.where(before, 1.0 / all_snaps, 0.0).astype(jnp.bfloat16)
    integral = integral_of(table, picks, upper, terms)

    increment = (series[:targets] - series[:targets, :, :1]).astype(jnp.bfloat16)
    contract = (((1, 2), (1, 2)), ((), ()))
    gram_part = lax.dot_general(integral, integral, contract, preferred_element_type=jnp.float32)
    cross_part = lax.dot_general(increment, integral, contract, preferred_element_type=jnp.float32)

    row_span = terms // point_devices
    col_span = terms // time_devices
    blocks = gram_part.reshape(point_devices, row_span, time_devices, col_span)
    blocks = jnp.transpose(blocks, (0, 2, 1, 3)).reshape(point_devices, time_devices, -1)
    cross_blocks = jnp.transpose(cross_part.reshape(targets, point_devices, row_span), (1, 0, 2))
    cross_blocks = jnp.broadcast_to(
        cross_blocks.reshape(point_devices, 1, -1), (point_devices, time_devices, targets * row_span)
    )
    packed = jnp.concatenate([blocks, cross_blocks], axis=2)
    mine = lax.psum_scatter(packed, "pts", scatter_dimension=0, tiled=True)[0]
    mine = lax.psum_scatter(mine, "tm", scatter_dimension=0, tiled=True)
    norm = jnp.float32(1.0 / (all_snaps * points * point_devices))
    mine = mine[0] * norm
    gram_own = mine[: row_span * col_span].reshape(row_span, col_span)
    cross_own = mine[row_span * col_span :].reshape(targets, row_span)
    return (gram_own, cross_own)


def solution(mesh):
    return jax.shard_map(
        shards,
        mesh=mesh,
        in_specs=(P(None, "tm", "pts"), P("pts"), P()),
        out_specs=(P("pts", "tm"), P(None, "pts")),
        check_vma=False,
    )
```

```python
import jax
import jax.numpy as jnp
from jax import lax
from jax.experimental import pallas as pl
from jax.experimental.pallas import tpu as pltpu
from jax.sharding import PartitionSpec as P


def factor_indices(exponents):
    running = jnp.cumsum(exponents, axis=1)
    picks = [jnp.sum((running <= j).astype(jnp.int32), axis=1) for j in range(3)]
    squared_last = (picks[1] == picks[2]) & (picks[0] != picks[1])
    ordered = [
        jnp.where(squared_last, picks[1], picks[0]),
        jnp.where(squared_last, picks[2], picks[1]),
        jnp.where(squared_last, picks[0], picks[2]),
    ]
    return jnp.stack(ordered)


def integral_kernel(picks_ref, table_ref, upper_ref, out_ref, high_ref, middle_ref, low_ref):
    block = pl.program_id(0)
    own = table_ref.shape[1]
    count = out_ref.shape[0] // own
    for j in range(count):
        term = block * count + j
        theta = (table_ref[picks_ref[0, term]] * table_ref[picks_ref[1, term]]) * table_ref[
            picks_ref[2, term]
        ]
        high = theta.astype(jnp.bfloat16)
        rest = theta - high.astype(jnp.float32)
        middle = rest.astype(jnp.bfloat16)
        low = (rest - middle.astype(jnp.float32)).astype(jnp.bfloat16)
        rows = pl.ds(j * own, own)
        high_ref[rows, :] = high
        middle_ref[rows, :] = middle
        low_ref[rows, :] = low
    upper = upper_ref[...]
    out = jnp.dot(high_ref[...], upper, preferred_element_type=jnp.float32)
    out = out + jnp.dot(middle_ref[...], upper, preferred_element_type=jnp.float32)
    out = out + jnp.dot(low_ref[...], upper, preferred_element_type=jnp.float32)
    out_ref[...] = out.astype(jnp.bfloat16)


def integral_of(table, picks, upper, terms, per_step=16):
    width, own, snaps = table.shape
    rows = per_step * own
    return pl.pallas_call(
        integral_kernel,
        out_shape=jax.ShapeDtypeStruct((terms * own, snaps), jnp.bfloat16),
        grid_spec=pltpu.PrefetchScalarGridSpec(
            num_scalar_prefetch=1,
            grid=(terms // per_step,),
            in_specs=[
                pl.BlockSpec((width, own, snaps), lambda i, picks: (0, 0, 0)),
                pl.BlockSpec((snaps, snaps), lambda i, picks: (0, 0)),
            ],
            out_specs=pl.BlockSpec((rows, snaps), lambda i, picks: (i, 0)),
            scratch_shapes=[pltpu.VMEM((rows, snaps), jnp.bfloat16) for _ in range(3)],
        ),
        compiler_params=pltpu.CompilerParams(dimension_semantics=("arbitrary",)),
    )(picks, table, upper).reshape(terms, own, snaps)


def halve(value, axis, bit, dim):
    size = lax.axis_size(axis)
    mine = (lax.axis_index(axis) // (1 << bit)) % 2
    kept = lax.dynamic_index_in_dim(value, mine, dim, keepdims=False)
    sent = lax.dynamic_index_in_dim(value, 1 - mine, dim, keepdims=False)
    pairs = [(i, i ^ (1 << bit)) for i in range(size)]
    return kept + lax.ppermute(sent, axis, pairs)


def reduce_scatter(packed, row_devices, col_devices):
    width = packed.shape[-1]
    row_bits = row_devices.bit_length() - 1
    col_bits = col_devices.bit_length() - 1
    value = packed.reshape((2,) * (row_bits + col_bits) + (width,))
    rounds = [("tm", 0)] + [("pts", b) for b in range(row_bits)] + [("tm", b) for b in range(1, col_bits)]
    names = [("pts", row_bits - 1 - d) for d in range(row_bits)] + [("tm", col_bits - 1 - d) for d in range(col_bits)]
    for axis, bit in rounds:
        dim = names.index((axis, bit))
        value = halve(value, axis, bit, dim)
        names.pop(dim)
    return value


def shards(base_grid, sample_index, exponents):
    fields, snaps, unused_cells = base_grid.shape
    points = sample_index.shape[0]
    terms = exponents.shape[0]
    targets = 3
    time_devices = lax.axis_size("tm")
    point_devices = lax.axis_size("pts")
    all_snaps = snaps * time_devices
    own = points // time_devices

    sampled = jnp.take(base_grid, sample_index, axis=2)
    sampled = lax.all_to_all(sampled, "tm", 2, 1, tiled=True)
    series = jnp.transpose(sampled, (0, 2, 1))
    ones = jnp.ones((1, own, all_snaps), jnp.float32)
    table = jnp.concatenate([series, ones], axis=0)

    picks = factor_indices(exponents)
    before = jnp.arange(all_snaps)[:, None] < jnp.arange(all_snaps)[None, :]
    upper = jnp.where(before, 1.0 / all_snaps, 0.0).astype(jnp.bfloat16)
    integral = integral_of(table, picks, upper, terms)

    increment = (series[:targets] - series[:targets, :, :1]).astype(jnp.bfloat16)
    contract = (((1, 2), (1, 2)), ((), ()))
    gram_part = lax.dot_general(integral, integral, contract, preferred_element_type=jnp.float32)
    cross_part = lax.dot_general(increment, integral, contract, preferred_element_type=jnp.float32)

    row_span = terms // point_devices
    col_span = terms // time_devices
    blocks = gram_part.reshape(point_devices, row_span, time_devices, col_span)
    blocks = jnp.transpose(blocks, (0, 2, 1, 3)).reshape(point_devices, time_devices, -1)
    cross_blocks = jnp.transpose(cross_part.reshape(targets, point_devices, row_span), (1, 0, 2))
    cross_blocks = jnp.broadcast_to(
        cross_blocks.reshape(point_devices, 1, -1), (point_devices, time_devices, targets * row_span)
    )
    packed = jnp.concatenate([blocks, cross_blocks], axis=2)
    mine = reduce_scatter(packed, point_devices, time_devices)
    norm = jnp.float32(1.0 / (all_snaps * points * point_devices))
    mine = mine * norm
    gram_own = mine[: row_span * col_span].reshape(row_span, col_span)
    cross_own = mine[row_span * col_span :].reshape(targets, row_span)
    return (gram_own, cross_own)


def solution(mesh):
    return jax.shard_map(
        shards,
        mesh=mesh,
        in_specs=(P(None, "tm", "pts"), P("pts"), P()),
        out_specs=(P("pts", "tm"), P(None, "pts")),
        check_vma=False,
    )
```

```python
import jax
import jax.numpy as jnp
from jax import lax
from jax.experimental import pallas as pl
from jax.experimental.pallas import tpu as pltpu
from jax.sharding import PartitionSpec as P

TARGETS = 3


def factor_indices(exponents):
    running = jnp.cumsum(exponents, axis=1)
    picks = [jnp.sum((running <= j).astype(jnp.int32), axis=1) for j in range(3)]
    squared_last = (picks[1] == picks[2]) & (picks[0] != picks[1])
    ordered = [
        jnp.where(squared_last, picks[1], picks[0]),
        jnp.where(squared_last, picks[2], picks[1]),
        jnp.where(squared_last, picks[0], picks[2]),
    ]
    return jnp.stack(ordered)


def integral_kernel(picks_ref, table_ref, upper_ref, out_ref, high_ref, middle_ref, low_ref):
    block = pl.program_id(0)
    own = table_ref.shape[1]
    count = out_ref.shape[0] // own

    @pl.when(block < pl.num_programs(0) - 1)
    def _():
        for j in range(count):
            term = block * count + j
            theta = (table_ref[picks_ref[0, term]] * table_ref[picks_ref[1, term]]) * table_ref[
                picks_ref[2, term]
            ]
            high = theta.astype(jnp.bfloat16)
            rest = theta - high.astype(jnp.float32)
            middle = rest.astype(jnp.bfloat16)
            low = (rest - middle.astype(jnp.float32)).astype(jnp.bfloat16)
            rows = pl.ds(j * own, own)
            high_ref[rows, :] = high
            middle_ref[rows, :] = middle
            low_ref[rows, :] = low
        upper = upper_ref[...]
        out = jnp.dot(high_ref[...], upper, preferred_element_type=jnp.float32)
        out = out + jnp.dot(middle_ref[...], upper, preferred_element_type=jnp.float32)
        out = out + jnp.dot(low_ref[...], upper, preferred_element_type=jnp.float32)
        out_ref[...] = out.astype(jnp.bfloat16)

    @pl.when(block == pl.num_programs(0) - 1)
    def _():
        for j in range(count):
            rows = pl.ds(j * own, own)
            if j < TARGETS:
                velocity = table_ref[j]
                out_ref[rows, :] = (velocity - velocity[:, :1]).astype(jnp.bfloat16)
            else:
                out_ref[rows, :] = jnp.zeros((own, out_ref.shape[1]), jnp.bfloat16)


def integral_of(table, picks, upper, terms, per_step=16):
    width, own, snaps = table.shape
    rows = per_step * own
    return pl.pallas_call(
        integral_kernel,
        out_shape=jax.ShapeDtypeStruct(((terms + per_step) * own, snaps), jnp.bfloat16),
        grid_spec=pltpu.PrefetchScalarGridSpec(
            num_scalar_prefetch=1,
            grid=(terms // per_step + 1,),
            in_specs=[
                pl.BlockSpec((width, own, snaps), lambda i, picks: (0, 0, 0)),
                pl.BlockSpec((snaps, snaps), lambda i, picks: (0, 0)),
            ],
            out_specs=pl.BlockSpec((rows, snaps), lambda i, picks: (i, 0)),
            scratch_shapes=[pltpu.VMEM((rows, snaps), jnp.bfloat16) for _ in range(3)],
        ),
        compiler_params=pltpu.CompilerParams(dimension_semantics=("arbitrary",)),
    )(picks, table, upper).reshape(terms + per_step, own, snaps)


def halve(value, axis, bit, dim):
    size = lax.axis_size(axis)
    mine = (lax.axis_index(axis) // (1 << bit)) % 2
    kept = lax.dynamic_index_in_dim(value, mine, dim, keepdims=False)
    sent = lax.dynamic_index_in_dim(value, 1 - mine, dim, keepdims=False)
    pairs = [(i, i ^ (1 << bit)) for i in range(size)]
    return kept + lax.ppermute(sent, axis, pairs)


def reduce_scatter(packed, row_devices, col_devices):
    width = packed.shape[-1]
    row_bits = row_devices.bit_length() - 1
    col_bits = col_devices.bit_length() - 1
    value = packed.reshape((2,) * (row_bits + col_bits) + (width,))
    rounds = [("tm", 0)] + [("pts", b) for b in range(row_bits)] + [("tm", b) for b in range(1, col_bits)]
    names = [("pts", row_bits - 1 - d) for d in range(row_bits)] + [("tm", col_bits - 1 - d) for d in range(col_bits)]
    for axis, bit in rounds:
        dim = names.index((axis, bit))
        value = halve(value, axis, bit, dim)
        names.pop(dim)
    return value


def shards(base_grid, sample_index, exponents):
    fields, snaps, unused_cells = base_grid.shape
    points = sample_index.shape[0]
    terms = exponents.shape[0]
    targets = 3
    time_devices = lax.axis_size("tm")
    point_devices = lax.axis_size("pts")
    all_snaps = snaps * time_devices
    own = points // time_devices

    sampled = jnp.take(base_grid, sample_index, axis=2)
    sampled = lax.all_to_all(sampled, "tm", 2, 1, tiled=True)
    series = jnp.transpose(sampled, (0, 2, 1))
    ones = jnp.ones((1, own, all_snaps), jnp.float32)
    table = jnp.concatenate([series, ones], axis=0)

    picks = factor_indices(exponents)
    before = jnp.arange(all_snaps)[:, None] < jnp.arange(all_snaps)[None, :]
    upper = jnp.where(before, 1.0 / all_snaps, 0.0).astype(jnp.bfloat16)
    integral = integral_of(table, picks, upper, terms)

    contract = (((1, 2), (1, 2)), ((), ()))
    products = lax.dot_general(integral, integral, contract, preferred_element_type=jnp.float32)
    gram_part = products[:terms, :terms]
    cross_part = products[terms : terms + targets, :terms]

    row_span = terms // point_devices
    col_span = terms // time_devices
    blocks = gram_part.reshape(point_devices, row_span, time_devices, col_span)
    blocks = jnp.transpose(blocks, (0, 2, 1, 3)).reshape(point_devices, time_devices, -1)
    cross_blocks = jnp.transpose(cross_part.reshape(targets, point_devices, row_span), (1, 0, 2))
    cross_blocks = jnp.broadcast_to(
        cross_blocks.reshape(point_devices, 1, -1), (point_devices, time_devices, targets * row_span)
    )
    packed = jnp.concatenate([blocks, cross_blocks], axis=2)
    mine = reduce_scatter(packed, point_devices, time_devices)
    norm = jnp.float32(1.0 / (all_snaps * points * point_devices))
    mine = mine * norm
    gram_own = mine[: row_span * col_span].reshape(row_span, col_span)
    cross_own = mine[row_span * col_span :].reshape(targets, row_span)
    return (gram_own, cross_own)


def solution(mesh):
    return jax.shard_map(
        shards,
        mesh=mesh,
        in_specs=(P(None, "tm", "pts"), P("pts"), P()),
        out_specs=(P("pts", "tm"), P(None, "pts")),
        check_vma=False,
    )
```

```python
import jax
import jax.numpy as jnp
from jax import lax
from jax.experimental import pallas as pl
from jax.experimental.pallas import tpu as pltpu
from jax.sharding import PartitionSpec as P

TARGETS = 3


def factor_indices(exponents):
    running = jnp.cumsum(exponents, axis=1)
    picks = [jnp.sum((running <= j).astype(jnp.int32), axis=1) for j in range(3)]
    squared_last = (picks[1] == picks[2]) & (picks[0] != picks[1])
    ordered = [
        jnp.where(squared_last, picks[1], picks[0]),
        jnp.where(squared_last, picks[2], picks[1]),
        jnp.where(squared_last, picks[0], picks[2]),
    ]
    return jnp.stack(ordered)


def integral_kernel(picks_ref, table_ref, upper_ref, out_ref, high_ref, middle_ref, low_ref):
    block = pl.program_id(0)
    own = table_ref.shape[1]
    count = out_ref.shape[0] // own

    @pl.when(block < pl.num_programs(0) - 1)
    def _():
        for j in range(count):
            term = block * count + j
            theta = (table_ref[picks_ref[0, term]] * table_ref[picks_ref[1, term]]) * table_ref[
                picks_ref[2, term]
            ]
            high = theta.astype(jnp.bfloat16)
            rest = theta - high.astype(jnp.float32)
            middle = rest.astype(jnp.bfloat16)
            low = (rest - middle.astype(jnp.float32)).astype(jnp.bfloat16)
            rows = pl.ds(j * own, own)
            high_ref[rows, :] = high
            middle_ref[rows, :] = middle
            low_ref[rows, :] = low
        upper = upper_ref[...]
        out = jnp.dot(high_ref[...], upper, preferred_element_type=jnp.float32)
        out = out + jnp.dot(middle_ref[...], upper, preferred_element_type=jnp.float32)
        out = out + jnp.dot(low_ref[...], upper, preferred_element_type=jnp.float32)
        out_ref[...] = out.astype(jnp.bfloat16)

    @pl.when(block == pl.num_programs(0) - 1)
    def _():
        for j in range(count):
            rows = pl.ds(j * own, own)
            if j < TARGETS:
                velocity = table_ref[j]
                out_ref[rows, :] = (velocity - velocity[:, :1]).astype(jnp.bfloat16)
            else:
                out_ref[rows, :] = jnp.zeros((own, out_ref.shape[1]), jnp.bfloat16)


def integral_of(table, picks, upper, terms, per_step=16):
    width, own, snaps = table.shape
    rows = per_step * own
    return pl.pallas_call(
        integral_kernel,
        out_shape=jax.ShapeDtypeStruct(((terms + per_step) * own, snaps), jnp.bfloat16),
        grid_spec=pltpu.PrefetchScalarGridSpec(
            num_scalar_prefetch=1,
            grid=(terms // per_step + 1,),
            in_specs=[
                pl.BlockSpec((width, own, snaps), lambda i, picks: (0, 0, 0)),
                pl.BlockSpec((snaps, snaps), lambda i, picks: (0, 0)),
            ],
            out_specs=pl.BlockSpec((rows, snaps), lambda i, picks: (i, 0)),
            scratch_shapes=[pltpu.VMEM((rows, snaps), jnp.bfloat16) for _ in range(3)],
        ),
        compiler_params=pltpu.CompilerParams(dimension_semantics=("arbitrary",)),
    )(picks, table, upper).reshape(terms + per_step, own, snaps)


def halve(value, axis, bit, dim):
    size = lax.axis_size(axis)
    mine = (lax.axis_index(axis) // (1 << bit)) % 2
    kept = lax.dynamic_index_in_dim(value, mine, dim, keepdims=False)
    sent = lax.dynamic_index_in_dim(value, 1 - mine, dim, keepdims=False)
    pairs = [(i, i ^ (1 << bit)) for i in range(size)]
    return kept + lax.ppermute(sent, axis, pairs)


def reduce_scatter(packed, row_devices, col_devices):
    width = packed.shape[-1]
    row_bits = row_devices.bit_length() - 1
    col_bits = col_devices.bit_length() - 1
    value = packed.reshape((2,) * (row_bits + col_bits) + (width,))
    rounds = [("tm", 0)] + [("pts", b) for b in range(row_bits)] + [("tm", b) for b in range(1, col_bits)]
    names = [("pts", row_bits - 1 - d) for d in range(row_bits)] + [("tm", col_bits - 1 - d) for d in range(col_bits)]
    for axis, bit in rounds:
        dim = names.index((axis, bit))
        value = halve(value, axis, bit, dim)
        names.pop(dim)
    return value


def shards(base_grid, sample_index, exponents):
    fields, snaps, unused_cells = base_grid.shape
    points = sample_index.shape[0]
    terms = exponents.shape[0]
    targets = 3
    time_devices = lax.axis_size("tm")
    point_devices = lax.axis_size("pts")
    all_snaps = snaps * time_devices
    own = points // time_devices

    cells = base_grid.shape[2]
    grid = base_grid.reshape(fields * snaps, cells)
    grid_high = grid.astype(jnp.bfloat16)
    grid_rest = grid - grid_high.astype(jnp.float32)
    grid_middle = grid_rest.astype(jnp.bfloat16)
    grid_low = (grid_rest - grid_middle.astype(jnp.float32)).astype(jnp.bfloat16)
    pick = (jnp.arange(cells)[:, None] == sample_index[None, :]).astype(jnp.bfloat16)
    sampled = (
        jnp.dot(grid_high, pick, preferred_element_type=jnp.float32)
        + jnp.dot(grid_middle, pick, preferred_element_type=jnp.float32)
        + jnp.dot(grid_low, pick, preferred_element_type=jnp.float32)
    )
    outgoing = jnp.transpose(sampled.reshape(fields, snaps, time_devices, own), (2, 0, 3, 1))
    incoming = lax.all_to_all(outgoing, "tm", 0, 0, tiled=True)
    series = jnp.transpose(incoming, (1, 2, 0, 3)).reshape(fields, own, all_snaps)
    ones = jnp.ones((1, own, all_snaps), jnp.float32)
    table = jnp.concatenate([series, ones], axis=0)

    picks = factor_indices(exponents)
    before = jnp.arange(all_snaps)[:, None] < jnp.arange(all_snaps)[None, :]
    upper = jnp.where(before, 1.0 / all_snaps, 0.0).astype(jnp.bfloat16)
    integral = integral_of(table, picks, upper, terms)

    contract = (((1, 2), (1, 2)), ((), ()))
    products = lax.dot_general(integral, integral, contract, preferred_element_type=jnp.float32)
    gram_part = products[:terms, :terms]
    cross_part = products[terms : terms + targets, :terms]

    row_span = terms // point_devices
    col_span = terms // time_devices
    blocks = gram_part.reshape(point_devices, row_span, time_devices, col_span)
    blocks = jnp.transpose(blocks, (0, 2, 1, 3)).reshape(point_devices, time_devices, -1)
    cross_blocks = jnp.transpose(cross_part.reshape(targets, point_devices, row_span), (1, 0, 2))
    cross_blocks = jnp.broadcast_to(
        cross_blocks.reshape(point_devices, 1, -1), (point_devices, time_devices, targets * row_span)
    )
    packed = jnp.concatenate([blocks, cross_blocks], axis=2)
    mine = reduce_scatter(packed, point_devices, time_devices)
    norm = jnp.float32(1.0 / (all_snaps * points * point_devices))
    mine = mine * norm
    gram_own = mine[: row_span * col_span].reshape(row_span, col_span)
    cross_own = mine[row_span * col_span :].reshape(targets, row_span)
    return (gram_own, cross_own)


def solution(mesh):
    return jax.shard_map(
        shards,
        mesh=mesh,
        in_specs=(P(None, "tm", "pts"), P("pts"), P()),
        out_specs=(P("pts", "tm"), P(None, "pts")),
        check_vma=False,
    )
```

```python
import jax
import jax.numpy as jnp
from jax import lax
from jax.experimental import pallas as pl
from jax.experimental.pallas import tpu as pltpu
from jax.sharding import PartitionSpec as P

TARGETS = 3


def factor_indices(exponents):
    running = jnp.cumsum(exponents, axis=1)
    picks = [jnp.sum((running <= j).astype(jnp.int32), axis=1) for j in range(3)]
    squared_last = (picks[1] == picks[2]) & (picks[0] != picks[1])
    ordered = [
        jnp.where(squared_last, picks[1], picks[0]),
        jnp.where(squared_last, picks[2], picks[1]),
        jnp.where(squared_last, picks[0], picks[2]),
    ]
    return jnp.stack(ordered)


def integral_kernel(picks_ref, table_ref, upper_ref, out_ref, high_ref, middle_ref, low_ref):
    block = pl.program_id(0)
    own = table_ref.shape[1]
    count = out_ref.shape[0] // own

    @pl.when(block < pl.num_programs(0) - 1)
    def _():
        for j in range(count):
            term = block * count + j
            theta = (table_ref[picks_ref[0, term]] * table_ref[picks_ref[1, term]]) * table_ref[
                picks_ref[2, term]
            ]
            high = theta.astype(jnp.bfloat16)
            rest = theta - high.astype(jnp.float32)
            middle = rest.astype(jnp.bfloat16)
            low = (rest - middle.astype(jnp.float32)).astype(jnp.bfloat16)
            rows = pl.ds(j * own, own)
            high_ref[rows, :] = high
            middle_ref[rows, :] = middle
            low_ref[rows, :] = low
        upper = upper_ref[...]
        out = jnp.dot(high_ref[...], upper, preferred_element_type=jnp.float32)
        out = out + jnp.dot(middle_ref[...], upper, preferred_element_type=jnp.float32)
        out = out + jnp.dot(low_ref[...], upper, preferred_element_type=jnp.float32)
        out_ref[...] = out.astype(jnp.bfloat16)

    @pl.when(block == pl.num_programs(0) - 1)
    def _():
        for j in range(count):
            rows = pl.ds(j * own, own)
            if j < TARGETS:
                velocity = table_ref[j]
                out_ref[rows, :] = (velocity - velocity[:, :1]).astype(jnp.bfloat16)
            else:
                out_ref[rows, :] = jnp.zeros((own, out_ref.shape[1]), jnp.bfloat16)


def integral_of(table, picks, upper, terms, per_step=32):
    width, own, snaps = table.shape
    rows = per_step * own
    return pl.pallas_call(
        integral_kernel,
        out_shape=jax.ShapeDtypeStruct(((terms + per_step) * own, snaps), jnp.bfloat16),
        grid_spec=pltpu.PrefetchScalarGridSpec(
            num_scalar_prefetch=1,
            grid=(terms // per_step + 1,),
            in_specs=[
                pl.BlockSpec((width, own, snaps), lambda i, picks: (0, 0, 0)),
                pl.BlockSpec((snaps, snaps), lambda i, picks: (0, 0)),
            ],
            out_specs=pl.BlockSpec((rows, snaps), lambda i, picks: (i, 0)),
            scratch_shapes=[pltpu.VMEM((rows, snaps), jnp.bfloat16) for _ in range(3)],
        ),
        compiler_params=pltpu.CompilerParams(dimension_semantics=("arbitrary",)),
    )(picks, table, upper).reshape(terms + per_step, own, snaps)


def halve(value, axis, bit, dim):
    size = lax.axis_size(axis)
    mine = (lax.axis_index(axis) // (1 << bit)) % 2
    kept = lax.dynamic_index_in_dim(value, mine, dim, keepdims=False)
    sent = lax.dynamic_index_in_dim(value, 1 - mine, dim, keepdims=False)
    pairs = [(i, i ^ (1 << bit)) for i in range(size)]
    return kept + lax.ppermute(sent, axis, pairs)


def reduce_scatter(packed, row_devices, col_devices):
    width = packed.shape[-1]
    row_bits = row_devices.bit_length() - 1
    col_bits = col_devices.bit_length() - 1
    value = packed.reshape((2,) * (row_bits + col_bits) + (width,))
    rounds = [("tm", 0)] + [("pts", b) for b in range(row_bits)] + [("tm", b) for b in range(1, col_bits)]
    names = [("pts", row_bits - 1 - d) for d in range(row_bits)] + [("tm", col_bits - 1 - d) for d in range(col_bits)]
    for axis, bit in rounds:
        dim = names.index((axis, bit))
        value = halve(value, axis, bit, dim)
        names.pop(dim)
    return value


def shards(base_grid, sample_index, exponents):
    fields, snaps, unused_cells = base_grid.shape
    points = sample_index.shape[0]
    terms = exponents.shape[0]
    targets = 3
    time_devices = lax.axis_size("tm")
    point_devices = lax.axis_size("pts")
    all_snaps = snaps * time_devices
    own = points // time_devices

    cells = base_grid.shape[2]
    grid = base_grid.reshape(fields * snaps, cells)
    grid_high = grid.astype(jnp.bfloat16)
    grid_rest = grid - grid_high.astype(jnp.float32)
    grid_middle = grid_rest.astype(jnp.bfloat16)
    grid_low = (grid_rest - grid_middle.astype(jnp.float32)).astype(jnp.bfloat16)
    pick = (jnp.arange(cells)[:, None] == sample_index[None, :]).astype(jnp.bfloat16)
    sampled = (
        jnp.dot(grid_high, pick, preferred_element_type=jnp.float32)
        + jnp.dot(grid_middle, pick, preferred_element_type=jnp.float32)
        + jnp.dot(grid_low, pick, preferred_element_type=jnp.float32)
    )
    outgoing = jnp.transpose(sampled.reshape(fields, snaps, time_devices, own), (2, 0, 3, 1))
    incoming = lax.all_to_all(outgoing, "tm", 0, 0, tiled=True)
    series = jnp.transpose(incoming, (1, 2, 0, 3)).reshape(fields, own, all_snaps)
    ones = jnp.ones((1, own, all_snaps), jnp.float32)
    table = jnp.concatenate([series, ones], axis=0)

    picks = factor_indices(exponents)
    before = jnp.arange(all_snaps)[:, None] < jnp.arange(all_snaps)[None, :]
    upper = jnp.where(before, 1.0 / all_snaps, 0.0).astype(jnp.bfloat16)
    integral = integral_of(table, picks, upper, terms)

    contract = (((1, 2), (1, 2)), ((), ()))
    products = lax.dot_general(integral, integral, contract, preferred_element_type=jnp.float32)
    gram_part = products[:terms, :terms]
    cross_part = products[terms : terms + targets, :terms]

    row_span = terms // point_devices
    col_span = terms // time_devices
    blocks = gram_part.reshape(point_devices, row_span, time_devices, col_span)
    blocks = jnp.transpose(blocks, (0, 2, 1, 3)).reshape(point_devices, time_devices, -1)
    cross_blocks = jnp.transpose(cross_part.reshape(targets, point_devices, row_span), (1, 0, 2))
    cross_blocks = jnp.broadcast_to(
        cross_blocks.reshape(point_devices, 1, -1), (point_devices, time_devices, targets * row_span)
    )
    packed = jnp.concatenate([blocks, cross_blocks], axis=2)
    mine = reduce_scatter(packed, point_devices, time_devices)
    norm = jnp.float32(1.0 / (all_snaps * points * point_devices))
    mine = mine * norm
    gram_own = mine[: row_span * col_span].reshape(row_span, col_span)
    cross_own = mine[row_span * col_span :].reshape(targets, row_span)
    return (gram_own, cross_own)


def solution(mesh):
    return jax.shard_map(
        shards,
        mesh=mesh,
        in_specs=(P(None, "tm", "pts"), P("pts"), P()),
        out_specs=(P("pts", "tm"), P(None, "pts")),
        check_vma=False,
    )
```

```python
import jax
import jax.numpy as jnp
from jax import lax
from jax.experimental import pallas as pl
from jax.experimental.pallas import tpu as pltpu
from jax.sharding import PartitionSpec as P

TARGETS = 3


def factor_indices(exponents):
    running = jnp.cumsum(exponents, axis=1)
    picks = [jnp.sum((running <= j).astype(jnp.int32), axis=1) for j in range(3)]
    squared_last = (picks[1] == picks[2]) & (picks[0] != picks[1])
    ordered = [
        jnp.where(squared_last, picks[1], picks[0]),
        jnp.where(squared_last, picks[2], picks[1]),
        jnp.where(squared_last, picks[0], picks[2]),
    ]
    return jnp.stack(ordered)


def integral_kernel(picks_ref, table_ref, upper_ref, out_ref, high_ref, middle_ref, low_ref):
    block = pl.program_id(0)
    own = table_ref.shape[1]
    count = out_ref.shape[0] // own

    @pl.when(block < pl.num_programs(0) - 1)
    def _():
        for j in range(count):
            term = block * count + j
            theta = (table_ref[picks_ref[0, term]] * table_ref[picks_ref[1, term]]) * table_ref[
                picks_ref[2, term]
            ]
            high = theta.astype(jnp.bfloat16)
            rest = theta - high.astype(jnp.float32)
            middle = rest.astype(jnp.bfloat16)
            low = (rest - middle.astype(jnp.float32)).astype(jnp.bfloat16)
            rows = pl.ds(j * own, own)
            high_ref[rows, :] = high
            middle_ref[rows, :] = middle
            low_ref[rows, :] = low
        upper = upper_ref[...]
        out = jnp.dot(high_ref[...], upper, preferred_element_type=jnp.float32)
        out = out + jnp.dot(middle_ref[...], upper, preferred_element_type=jnp.float32)
        out = out + jnp.dot(low_ref[...], upper, preferred_element_type=jnp.float32)
        out_ref[...] = out.astype(jnp.bfloat16)

    @pl.when(block == pl.num_programs(0) - 1)
    def _():
        for j in range(count):
            rows = pl.ds(j * own, own)
            if j < TARGETS:
                velocity = table_ref[j]
                out_ref[rows, :] = (velocity - velocity[:, :1]).astype(jnp.bfloat16)
            else:
                out_ref[rows, :] = jnp.zeros((own, out_ref.shape[1]), jnp.bfloat16)


def integral_of(table, picks, upper, terms, per_step=32):
    width, own, snaps = table.shape
    rows = per_step * own
    return pl.pallas_call(
        integral_kernel,
        out_shape=jax.ShapeDtypeStruct(((terms + per_step) * own, snaps), jnp.bfloat16),
        grid_spec=pltpu.PrefetchScalarGridSpec(
            num_scalar_prefetch=1,
            grid=(terms // per_step + 1,),
            in_specs=[
                pl.BlockSpec((width, own, snaps), lambda i, picks: (0, 0, 0)),
                pl.BlockSpec((snaps, snaps), lambda i, picks: (0, 0)),
            ],
            out_specs=pl.BlockSpec((rows, snaps), lambda i, picks: (i, 0)),
            scratch_shapes=[pltpu.VMEM((rows, snaps), jnp.bfloat16) for _ in range(3)],
        ),
        compiler_params=pltpu.CompilerParams(dimension_semantics=("arbitrary",)),
    )(picks, table, upper).reshape(terms + per_step, own, snaps)


def exchange(value, axis, bit, digits, dim):
    size = lax.axis_size(axis)
    mine = (lax.axis_index(axis) // (1 << bit)) % digits
    total = lax.dynamic_index_in_dim(value, mine, dim, keepdims=False)
    for offset in range(1, digits):
        sent = lax.dynamic_index_in_dim(value, jnp.bitwise_xor(mine, offset), dim, keepdims=False)
        pairs = [(i, i ^ (offset << bit)) for i in range(size)]
        total = total + lax.ppermute(sent, axis, pairs)
    return total


def reduce_scatter(packed, row_devices, col_devices):
    width = packed.shape[-1]
    row_bits = row_devices.bit_length() - 1
    col_bits = col_devices.bit_length() - 1
    value = packed.reshape((2,) * (row_bits + col_bits) + (width,))
    names = [("pts", row_bits - 1 - d) for d in range(row_bits)]
    names += [("tm", col_bits - 1 - d) for d in range(col_bits)]
    rounds = [("tm", 0, 1)] if col_bits else []
    for axis, low, bits in (("pts", 0, row_bits), ("tm", 1, col_bits)):
        for bit in range(low, bits, 2):
            rounds.append((axis, bit, min(2, bits - bit)))
    for axis, bit, count in rounds:
        dim = names.index((axis, bit + count - 1))
        shape = value.shape
        value = value.reshape(shape[:dim] + (1 << count,) + shape[dim + count :])
        value = exchange(value, axis, bit, 1 << count, dim)
        del names[dim : dim + count]
    return value


def shards(base_grid, sample_index, exponents):
    fields, snaps, unused_cells = base_grid.shape
    points = sample_index.shape[0]
    terms = exponents.shape[0]
    targets = 3
    time_devices = lax.axis_size("tm")
    point_devices = lax.axis_size("pts")
    all_snaps = snaps * time_devices
    own = points // time_devices

    cells = base_grid.shape[2]
    grid = base_grid.reshape(fields * snaps, cells)
    grid_high = grid.astype(jnp.bfloat16)
    grid_rest = grid - grid_high.astype(jnp.float32)
    grid_middle = grid_rest.astype(jnp.bfloat16)
    grid_low = (grid_rest - grid_middle.astype(jnp.float32)).astype(jnp.bfloat16)
    pick = (jnp.arange(cells)[:, None] == sample_index[None, :]).astype(jnp.bfloat16)
    sampled = (
        jnp.dot(grid_high, pick, preferred_element_type=jnp.float32)
        + jnp.dot(grid_middle, pick, preferred_element_type=jnp.float32)
        + jnp.dot(grid_low, pick, preferred_element_type=jnp.float32)
    )
    outgoing = jnp.transpose(sampled.reshape(fields, snaps, time_devices, own), (2, 0, 3, 1))
    incoming = lax.all_to_all(outgoing, "tm", 0, 0, tiled=True)
    series = jnp.transpose(incoming, (1, 2, 0, 3)).reshape(fields, own, all_snaps)
    ones = jnp.ones((1, own, all_snaps), jnp.float32)
    table = jnp.concatenate([series, ones], axis=0)

    picks = factor_indices(exponents)
    before = jnp.arange(all_snaps)[:, None] < jnp.arange(all_snaps)[None, :]
    upper = jnp.where(before, 1.0 / all_snaps, 0.0).astype(jnp.bfloat16)
    integral = integral_of(table, picks, upper, terms)

    contract = (((1, 2), (1, 2)), ((), ()))
    products = lax.dot_general(integral, integral, contract, preferred_element_type=jnp.float32)
    gram_part = products[:terms, :terms]
    cross_part = products[terms : terms + targets, :terms]

    row_span = terms // point_devices
    col_span = terms // time_devices
    blocks = gram_part.reshape(point_devices, row_span, time_devices, col_span)
    blocks = jnp.transpose(blocks, (0, 2, 1, 3)).reshape(point_devices, time_devices, -1)
    cross_blocks = jnp.transpose(cross_part.reshape(targets, point_devices, row_span), (1, 0, 2))
    cross_blocks = jnp.broadcast_to(
        cross_blocks.reshape(point_devices, 1, -1), (point_devices, time_devices, targets * row_span)
    )
    packed = jnp.concatenate([blocks, cross_blocks], axis=2)
    mine = reduce_scatter(packed, point_devices, time_devices)
    norm = jnp.float32(1.0 / (all_snaps * points * point_devices))
    mine = mine * norm
    gram_own = mine[: row_span * col_span].reshape(row_span, col_span)
    cross_own = mine[row_span * col_span :].reshape(targets, row_span)
    return (gram_own, cross_own)


def solution(mesh):
    return jax.shard_map(
        shards,
        mesh=mesh,
        in_specs=(P(None, "tm", "pts"), P("pts"), P()),
        out_specs=(P("pts", "tm"), P(None, "pts")),
        check_vma=False,
    )
```

```python
import jax
import jax.numpy as jnp
from jax import lax
from jax.experimental import pallas as pl
from jax.experimental.pallas import tpu as pltpu
from jax.sharding import PartitionSpec as P

TARGETS = 3


def factor_indices(exponents):
    running = jnp.cumsum(exponents, axis=1)
    picks = [jnp.sum((running <= j).astype(jnp.int32), axis=1) for j in range(3)]
    squared_last = (picks[1] == picks[2]) & (picks[0] != picks[1])
    ordered = [
        jnp.where(squared_last, picks[1], picks[0]),
        jnp.where(squared_last, picks[2], picks[1]),
        jnp.where(squared_last, picks[0], picks[2]),
    ]
    return jnp.stack(ordered)


def integral_kernel(picks_ref, table_ref, upper_ref, out_ref, high_ref, middle_ref, low_ref):
    block = pl.program_id(0)
    own = table_ref.shape[1]
    count = out_ref.shape[0] // own

    @pl.when(block < pl.num_programs(0) - 1)
    def _():
        for j in range(count):
            term = block * count + j
            theta = (table_ref[picks_ref[0, term]] * table_ref[picks_ref[1, term]]) * table_ref[
                picks_ref[2, term]
            ]
            high = theta.astype(jnp.bfloat16)
            rest = theta - high.astype(jnp.float32)
            middle = rest.astype(jnp.bfloat16)
            low = (rest - middle.astype(jnp.float32)).astype(jnp.bfloat16)
            rows = pl.ds(j * own, own)
            high_ref[rows, :] = high
            middle_ref[rows, :] = middle
            low_ref[rows, :] = low
        upper = upper_ref[...]
        out = jnp.dot(high_ref[...], upper, preferred_element_type=jnp.float32)
        out = out + jnp.dot(middle_ref[...], upper, preferred_element_type=jnp.float32)
        out = out + jnp.dot(low_ref[...], upper, preferred_element_type=jnp.float32)
        out_ref[...] = out.astype(jnp.bfloat16)

    @pl.when(block == pl.num_programs(0) - 1)
    def _():
        for j in range(count):
            rows = pl.ds(j * own, own)
            if j < TARGETS:
                velocity = table_ref[j]
                out_ref[rows, :] = (velocity - velocity[:, :1]).astype(jnp.bfloat16)
            else:
                out_ref[rows, :] = jnp.zeros((own, out_ref.shape[1]), jnp.bfloat16)


def integral_of(table, picks, upper, terms, per_step=32):
    width, own, snaps = table.shape
    rows = per_step * own
    return pl.pallas_call(
        integral_kernel,
        out_shape=jax.ShapeDtypeStruct(((terms + per_step) * own, snaps), jnp.bfloat16),
        grid_spec=pltpu.PrefetchScalarGridSpec(
            num_scalar_prefetch=1,
            grid=(terms // per_step + 1,),
            in_specs=[
                pl.BlockSpec((width, own, snaps), lambda i, picks: (0, 0, 0)),
                pl.BlockSpec((snaps, snaps), lambda i, picks: (0, 0)),
            ],
            out_specs=pl.BlockSpec((rows, snaps), lambda i, picks: (i, 0)),
            scratch_shapes=[pltpu.VMEM((rows, snaps), jnp.bfloat16) for _ in range(3)],
        ),
        compiler_params=pltpu.CompilerParams(dimension_semantics=("arbitrary",)),
    )(picks, table, upper).reshape(terms + per_step, own, snaps)


def swap_parts(outgoing, axis):
    size = lax.axis_size(axis)
    mine = lax.axis_index(axis)
    arrived = [lax.dynamic_index_in_dim(outgoing, mine, 0, keepdims=False)]
    for offset in range(1, size):
        sent = lax.dynamic_index_in_dim(outgoing, jnp.bitwise_xor(mine, offset), 0, keepdims=False)
        arrived.append(lax.ppermute(sent, axis, [(i, i ^ offset) for i in range(size)]))
    arrived = jnp.stack(arrived)
    return jnp.stack(
        [lax.dynamic_index_in_dim(arrived, jnp.bitwise_xor(mine, s), 0, keepdims=False) for s in range(size)]
    )


def exchange(value, axis, bit, digits, dim):
    size = lax.axis_size(axis)
    mine = (lax.axis_index(axis) // (1 << bit)) % digits
    total = lax.dynamic_index_in_dim(value, mine, dim, keepdims=False)
    for offset in range(1, digits):
        sent = lax.dynamic_index_in_dim(value, jnp.bitwise_xor(mine, offset), dim, keepdims=False)
        pairs = [(i, i ^ (offset << bit)) for i in range(size)]
        total = total + lax.ppermute(sent, axis, pairs)
    return total


def reduce_scatter(packed, row_devices, col_devices):
    width = packed.shape[-1]
    row_bits = row_devices.bit_length() - 1
    col_bits = col_devices.bit_length() - 1
    value = packed.reshape((2,) * (row_bits + col_bits) + (width,))
    names = [("pts", row_bits - 1 - d) for d in range(row_bits)]
    names += [("tm", col_bits - 1 - d) for d in range(col_bits)]
    rounds = [("tm", 0, 1)] if col_bits else []
    for axis, low, bits in (("pts", 0, row_bits), ("tm", 1, col_bits)):
        for bit in range(low, bits, 2):
            rounds.append((axis, bit, min(2, bits - bit)))
    for axis, bit, count in rounds:
        dim = names.index((axis, bit + count - 1))
        shape = value.shape
        value = value.reshape(shape[:dim] + (1 << count,) + shape[dim + count :])
        value = exchange(value, axis, bit, 1 << count, dim)
        del names[dim : dim + count]
    return value


def shards(base_grid, sample_index, exponents):
    fields, snaps, unused_cells = base_grid.shape
    points = sample_index.shape[0]
    terms = exponents.shape[0]
    targets = 3
    time_devices = lax.axis_size("tm")
    point_devices = lax.axis_size("pts")
    all_snaps = snaps * time_devices
    own = points // time_devices

    cells = base_grid.shape[2]
    grid = base_grid.reshape(fields * snaps, cells)
    grid_high = grid.astype(jnp.bfloat16)
    grid_rest = grid - grid_high.astype(jnp.float32)
    grid_middle = grid_rest.astype(jnp.bfloat16)
    grid_low = (grid_rest - grid_middle.astype(jnp.float32)).astype(jnp.bfloat16)
    pick = (jnp.arange(cells)[:, None] == sample_index[None, :]).astype(jnp.bfloat16)
    sampled = (
        jnp.dot(grid_high, pick, preferred_element_type=jnp.float32)
        + jnp.dot(grid_middle, pick, preferred_element_type=jnp.float32)
        + jnp.dot(grid_low, pick, preferred_element_type=jnp.float32)
    )
    outgoing = jnp.transpose(sampled.reshape(fields, snaps, time_devices, own), (2, 0, 3, 1))
    incoming = swap_parts(outgoing, "tm")
    series = jnp.transpose(incoming, (1, 2, 0, 3)).reshape(fields, own, all_snaps)
    ones = jnp.ones((1, own, all_snaps), jnp.float32)
    table = jnp.concatenate([series, ones], axis=0)

    picks = factor_indices(exponents)
    before = jnp.arange(all_snaps)[:, None] < jnp.arange(all_snaps)[None, :]
    upper = jnp.where(before, 1.0 / all_snaps, 0.0).astype(jnp.bfloat16)
    integral = integral_of(table, picks, upper, terms)

    contract = (((1, 2), (1, 2)), ((), ()))
    products = lax.dot_general(integral, integral, contract, preferred_element_type=jnp.float32)
    gram_part = products[:terms, :terms]
    cross_part = products[terms : terms + targets, :terms]

    row_span = terms // point_devices
    col_span = terms // time_devices
    blocks = gram_part.reshape(point_devices, row_span, time_devices, col_span)
    blocks = jnp.transpose(blocks, (0, 2, 1, 3)).reshape(point_devices, time_devices, -1)
    cross_blocks = jnp.transpose(cross_part.reshape(targets, point_devices, row_span), (1, 0, 2))
    cross_blocks = jnp.broadcast_to(
        cross_blocks.reshape(point_devices, 1, -1), (point_devices, time_devices, targets * row_span)
    )
    packed = jnp.concatenate([blocks, cross_blocks], axis=2)
    mine = reduce_scatter(packed, point_devices, time_devices)
    norm = jnp.float32(1.0 / (all_snaps * points * point_devices))
    mine = mine * norm
    gram_own = mine[: row_span * col_span].reshape(row_span, col_span)
    cross_own = mine[row_span * col_span :].reshape(targets, row_span)
    return (gram_own, cross_own)


def solution(mesh):
    return jax.shard_map(
        shards,
        mesh=mesh,
        in_specs=(P(None, "tm", "pts"), P("pts"), P()),
        out_specs=(P("pts", "tm"), P(None, "pts")),
        check_vma=False,
    )
```

```python
import jax
import jax.numpy as jnp
from jax import lax
from jax.experimental import pallas as pl
from jax.experimental.pallas import tpu as pltpu
from jax.sharding import PartitionSpec as P

TARGETS = 3


def factor_indices(exponents):
    running = jnp.cumsum(exponents, axis=1)
    picks = [jnp.sum((running <= j).astype(jnp.int32), axis=1) for j in range(3)]
    squared_last = (picks[1] == picks[2]) & (picks[0] != picks[1])
    ordered = [
        jnp.where(squared_last, picks[1], picks[0]),
        jnp.where(squared_last, picks[2], picks[1]),
        jnp.where(squared_last, picks[0], picks[2]),
    ]
    return jnp.stack(ordered)


def integral_kernel(picks_ref, table_ref, upper_ref, out_ref, high_ref, middle_ref, low_ref):
    block = pl.program_id(0)
    own = table_ref.shape[1]
    count = out_ref.shape[0] // own

    @pl.when(block < pl.num_programs(0) - 1)
    def _():
        for j in range(count):
            term = block * count + j
            theta = (table_ref[picks_ref[0, term]] * table_ref[picks_ref[1, term]]) * table_ref[
                picks_ref[2, term]
            ]
            high = theta.astype(jnp.bfloat16)
            rest = theta - high.astype(jnp.float32)
            middle = rest.astype(jnp.bfloat16)
            low = (rest - middle.astype(jnp.float32)).astype(jnp.bfloat16)
            rows = pl.ds(j * own, own)
            high_ref[rows, :] = high
            middle_ref[rows, :] = middle
            low_ref[rows, :] = low
        upper = upper_ref[...]
        out = jnp.dot(high_ref[...], upper, preferred_element_type=jnp.float32)
        out = out + jnp.dot(middle_ref[...], upper, preferred_element_type=jnp.float32)
        out = out + jnp.dot(low_ref[...], upper, preferred_element_type=jnp.float32)
        out_ref[...] = out.astype(jnp.bfloat16)

    @pl.when(block == pl.num_programs(0) - 1)
    def _():
        for j in range(count):
            rows = pl.ds(j * own, own)
            if j < TARGETS:
                velocity = table_ref[j]
                out_ref[rows, :] = (velocity - velocity[:, :1]).astype(jnp.bfloat16)
            else:
                out_ref[rows, :] = jnp.zeros((own, out_ref.shape[1]), jnp.bfloat16)


def integral_of(table, picks, upper, terms, per_step=32):
    width, own, snaps = table.shape
    rows = per_step * own
    return pl.pallas_call(
        integral_kernel,
        out_shape=jax.ShapeDtypeStruct(((terms + per_step) * own, snaps), jnp.bfloat16),
        grid_spec=pltpu.PrefetchScalarGridSpec(
            num_scalar_prefetch=1,
            grid=(terms // per_step + 1,),
            in_specs=[
                pl.BlockSpec((width, own, snaps), lambda i, picks: (0, 0, 0)),
                pl.BlockSpec((snaps, snaps), lambda i, picks: (0, 0)),
            ],
            out_specs=pl.BlockSpec((rows, snaps), lambda i, picks: (i, 0)),
            scratch_shapes=[pltpu.VMEM((rows, snaps), jnp.bfloat16) for _ in range(3)],
        ),
        compiler_params=pltpu.CompilerParams(dimension_semantics=("arbitrary",)),
    )(picks, table, upper).reshape(terms + per_step, own, snaps)


def exchange(value, axis, bit, digits, dim):
    size = lax.axis_size(axis)
    mine = (lax.axis_index(axis) // (1 << bit)) % digits
    total = lax.dynamic_index_in_dim(value, mine, dim, keepdims=False)
    for offset in range(1, digits):
        sent = lax.dynamic_index_in_dim(value, jnp.bitwise_xor(mine, offset), dim, keepdims=False)
        pairs = [(i, i ^ (offset << bit)) for i in range(size)]
        total = total + lax.ppermute(sent, axis, pairs)
    return total


def reduce_scatter(packed, row_devices, col_devices):
    width = packed.shape[-1]
    row_bits = row_devices.bit_length() - 1
    col_bits = col_devices.bit_length() - 1
    value = packed.reshape((2,) * (row_bits + col_bits) + (width,))
    names = [("pts", row_bits - 1 - d) for d in range(row_bits)]
    names += [("tm", col_bits - 1 - d) for d in range(col_bits)]
    first = min(2, col_bits)
    rounds = [("tm", 0, first)] if col_bits else []
    for axis, low, bits in (("pts", 0, row_bits), ("tm", first, col_bits)):
        for bit in range(low, bits, 2):
            rounds.append((axis, bit, min(2, bits - bit)))
    for axis, bit, count in rounds:
        dim = names.index((axis, bit + count - 1))
        shape = value.shape
        value = value.reshape(shape[:dim] + (1 << count,) + shape[dim + count :])
        value = exchange(value, axis, bit, 1 << count, dim)
        del names[dim : dim + count]
    return value


def shards(base_grid, sample_index, exponents):
    fields, snaps, unused_cells = base_grid.shape
    points = sample_index.shape[0]
    terms = exponents.shape[0]
    targets = 3
    time_devices = lax.axis_size("tm")
    point_devices = lax.axis_size("pts")
    all_snaps = snaps * time_devices
    own = points // time_devices

    cells = base_grid.shape[2]
    grid = base_grid.reshape(fields * snaps, cells)
    grid_high = grid.astype(jnp.bfloat16)
    grid_rest = grid - grid_high.astype(jnp.float32)
    grid_middle = grid_rest.astype(jnp.bfloat16)
    grid_low = (grid_rest - grid_middle.astype(jnp.float32)).astype(jnp.bfloat16)
    pick = (jnp.arange(cells)[:, None] == sample_index[None, :]).astype(jnp.bfloat16)
    sampled = (
        jnp.dot(grid_high, pick, preferred_element_type=jnp.float32)
        + jnp.dot(grid_middle, pick, preferred_element_type=jnp.float32)
        + jnp.dot(grid_low, pick, preferred_element_type=jnp.float32)
    )
    outgoing = jnp.transpose(sampled.reshape(fields, snaps, time_devices, own), (2, 0, 3, 1))
    incoming = lax.all_to_all(outgoing, "tm", 0, 0, tiled=True)
    series = jnp.transpose(incoming, (1, 2, 0, 3)).reshape(fields, own, all_snaps)
    ones = jnp.ones((1, own, all_snaps), jnp.float32)
    table = jnp.concatenate([series, ones], axis=0)

    picks = factor_indices(exponents)
    before = jnp.arange(all_snaps)[:, None] < jnp.arange(all_snaps)[None, :]
    upper = jnp.where(before, 1.0 / all_snaps, 0.0).astype(jnp.bfloat16)
    integral = integral_of(table, picks, upper, terms)

    contract = (((1, 2), (1, 2)), ((), ()))
    products = lax.dot_general(integral, integral, contract, preferred_element_type=jnp.float32)
    gram_part = products[:terms, :terms]
    cross_part = products[terms : terms + targets, :terms]

    row_span = terms // point_devices
    col_span = terms // time_devices
    blocks = gram_part.reshape(point_devices, row_span, time_devices, col_span)
    blocks = jnp.transpose(blocks, (0, 2, 1, 3)).reshape(point_devices, time_devices, -1)
    cross_blocks = jnp.transpose(cross_part.reshape(targets, point_devices, row_span), (1, 0, 2))
    cross_blocks = jnp.broadcast_to(
        cross_blocks.reshape(point_devices, 1, -1), (point_devices, time_devices, targets * row_span)
    )
    packed = jnp.concatenate([blocks, cross_blocks], axis=2)
    mine = reduce_scatter(packed, point_devices, time_devices)
    norm = jnp.float32(1.0 / (all_snaps * points * point_devices))
    mine = mine * norm
    gram_own = mine[: row_span * col_span].reshape(row_span, col_span)
    cross_own = mine[row_span * col_span :].reshape(targets, row_span)
    return (gram_own, cross_own)


def solution(mesh):
    return jax.shard_map(
        shards,
        mesh=mesh,
        in_specs=(P(None, "tm", "pts"), P("pts"), P()),
        out_specs=(P("pts", "tm"), P(None, "pts")),
        check_vma=False,
    )
```
